128 devices in a mesh: blk: 32 (over x, z, y_hi), sub: 4 (over y_lo, core).
Axes of the slice: x: 4, y: 4 (y_hi: 2, y_lo: 2; y = y_hi * 2 + y_lo), z: 4, core: 2. Of those that a mesh axis runs over, the one named last changes fastest.
Arguments:
- phase: float32 [6, 131072], P(None, ('blk', 'sub')), may hold values from -6 to 6
- derivs: float32 [6, 131072], P(None, ('blk', 'sub')), may hold values from -6 to 6
- mass: float32 [131072], P(('blk', 'sub')), may hold values from 1.5258789e-05 to 0.00024414062
- elapsed: float32 [131072], P(('blk', 'sub')), may hold values from 0.05 to 0.5
- active_slots: int32 [3, 8192], P(None, ('blk', 'sub')), may hold values from 0 to 1023, as said below
- active_counts: int32 [3, 128], P(None, ('blk', 'sub')), may hold values from 33 to 64, as said below
Outputs:
- new_phase: float32 [6, 131072], P(None, ('blk', 'sub'))
- new_derivs: float32 [6, 131072], P(None, ('blk', 'sub'))
- active_forces: float32 [6, 3, 8192], P(None, None, ('blk', 'sub'))
The draws below stay inside these ranges and needn't reach their ends.
Inputs may be any that keep to these rules, and one draw needn't show every extreme that they name: `active_slots`: on each device the 192 entries, padding included, are distinct slots of that device's own stars. `active_counts`: in every level some device's list is full.
All inputs are finite; a program needn't handle non-finite values.
Results may differ from the reference program's by a relative error of at most 0.00027.
Values sent between devices are 32-bit elements; how exact they have to be, the bound alone decides.
No kernel may reach another device: no remote copies, remote signals or barrier semaphores. Data moves between devices by JAX's collectives and lax.ppermute only.
A program may use at most 64 MiB of HBM per device.

```python
import math
import jax
import jax.numpy as jnp
from jax import lax

PDEV = 1024
LEVELS = 3
LCAP = 64
NSTARS = 131072
N_BLK = 32
N_SUB = 4


def draw_active_slots(key, part):
    n_dev = NSTARS // PDEV
    dev_keys = jax.random.split(key, n_dev)
    shuffled = jax.vmap(lambda one_key: jax.random.permutation(one_key, PDEV)[:LEVELS * LCAP])(dev_keys)
    shaped = shuffled.reshape(n_dev, LEVELS, LCAP).transpose(1, 0, 2).reshape(LEVELS, n_dev * LCAP)
    return shaped.astype(jnp.int32)


def draw_active_counts(key, part):
    n_dev = NSTARS // PDEV
    key_one, key_two, key_three = jax.random.split(jax.random.fold_in(key, 7), 3)
    first = jax.random.randint(key_one, (LEVELS, n_dev), 0, LCAP)
    second = jax.random.randint(key_two, (LEVELS, n_dev), 0, LCAP)
    counts = LCAP // 2 + first * second // (2 * LCAP) + 1
    counts = jnp.minimum(counts, LCAP)
    busiest = jax.random.randint(key_three, (LEVELS, 1), 0, n_dev)
    column = jnp.arange(n_dev, dtype=jnp.int32)[None, :]
    return jnp.where(column == busiest, LCAP, counts).astype(jnp.int32)


def level_of(rng, shape, cuts, smallest, largest):
    def one(dim, shards_of):
        heights = jax.random.uniform(jax.random.fold_in(jax.random.fold_in(rng, 6), dim), (shards_of,), jnp.float32, smallest / len(cuts), largest / len(cuts))
        return jnp.repeat(jnp.exp(heights), shape[dim] // shards_of).reshape((-1,) + (1,) * (len(shape) - dim - 1))

    factor_of = one(*cuts[0])
    for cut in cuts[1:]:
        factor_of = factor_of * one(*cut)
    return factor_of


def noise(rng, dims, deviation, reach, cuts=(), kind=jnp.bfloat16):
    array = deviation * jax.random.normal(rng, dims, jnp.float32)
    if cuts:
        array = array * level_of(rng, dims, cuts, -0.22, 0.18)
    return jnp.clip(array, -reach, reach).astype(kind)


def setup_inputs(seed: int = 0) -> dict:
    seeds = jax.random.split(jax.random.key(seed), 7)
    phase = noise(seeds[0], (6, NSTARS), 1.0, 6.0, ((1, 128),), jnp.float32)
    derivs = noise(seeds[1], (6, NSTARS), 1.0, 6.0, ((1, 128),), jnp.float32)
    mass = jnp.clip(jnp.exp(math.log(0.00024414062) - 2.7725887 * jax.random.uniform(seeds[2], (NSTARS,), jnp.float32) ** level_of(seeds[2], (NSTARS,), ((0, 128),), -0.2, 0.2)), 1.52587890625e-05, 0.00024414062)
    elapsed = jnp.clip(jnp.exp(math.log(0.5) - 2.3025851 * jax.random.uniform(seeds[3], (NSTARS,), jnp.float32) ** level_of(seeds[3], (NSTARS,), ((0, 128),), -0.2, 0.2)), 0.05, 0.5)
    active_slots = draw_active_slots(jax.random.fold_in(seeds[6], 71), 0)
    active_counts = draw_active_counts(jax.random.fold_in(seeds[6], 71), 0)
    return {"phase": phase, "derivs": derivs, "mass": mass, "elapsed": elapsed, "active_slots": active_slots, "active_counts": active_counts}


SOFTEN_SQ = 0.0025

def predict(phase, derivs, elapsed):
    t_now = elapsed[None, :]
    pos_pred = phase[:3] + t_now * phase[3:] + t_now * t_now / 2.0 * derivs[:3] + t_now * t_now * t_now / 6.0 * derivs[3:]
    vel_pred = phase[3:] + t_now * derivs[:3] + t_now * t_now / 2.0 * derivs[3:]
    return (pos_pred, vel_pred)

def pair_terms(i_pos, i_vel, j_pos, j_vel, j_mass):
    offset = j_pos[:, None, :] - i_pos[:, :, None]
    rel_vel = j_vel[:, None, :] - i_vel[:, :, None]
    dist_sq = lax.optimization_barrier(jnp.sum(offset * offset, axis=0)) + SOFTEN_SQ
    inverse = lax.rsqrt(dist_sq)
    weight = j_mass[None, :] * inverse * inverse * inverse
    radial = 3.0 * lax.optimization_barrier(jnp.sum(offset * rel_vel, axis=0)) / dist_sq
    accel_sum = lax.optimization_barrier(jnp.sum(weight[None] * offset, axis=2))
    jerk_sum = lax.optimization_barrier(jnp.sum(weight[None] * (rel_vel - radial[None] * offset), axis=2))
    return (accel_sum, jerk_sum)

def correct(pred_rows, old_rows, step_len, new_forces):
    diff_acc = old_rows[:3] - new_forces[:3]
    step_row = step_len[None, :]
    term_two = -6.0 * diff_acc - step_row * (4.0 * old_rows[3:] + 2.0 * new_forces[3:])
    term_three = 12.0 * diff_acc + 6.0 * step_row * (old_rows[3:] + new_forces[3:])
    pos_new = pred_rows[:3] + step_row * step_row * (term_two / 24.0 + term_three / 120.0)
    vel_new = pred_rows[3:] + step_row * (term_two / 6.0 + term_three / 24.0)
    return jnp.concatenate([pos_new, vel_new], axis=0)

def reference(phase, derivs, mass, elapsed, active_slots, active_counts):
    pred_pos, pred_vel = predict(phase, derivs, elapsed)
    n_dev = N_BLK * N_SUB
    col_idx = jnp.arange(n_dev * LCAP, dtype=jnp.int32)
    owner_base = col_idx // LCAP * PDEV
    global_rows = (active_slots + owner_base[None, :]).astype(jnp.int32)
    is_live = (col_idx % LCAP)[None, :] < jnp.repeat(active_counts, LCAP, axis=1)
    flat_rows = global_rows.reshape(-1)
    i_pos = pred_pos[:, flat_rows]
    i_vel = pred_vel[:, flat_rows]
    n_rows = flat_rows.shape[0]
    tiled_pos = i_pos.reshape(3, n_rows // LCAP, LCAP).transpose(1, 0, 2)
    tiled_vel = i_vel.reshape(3, n_rows // LCAP, LCAP).transpose(1, 0, 2)
    j_pos = pred_pos.reshape(3, N_BLK, N_SUB * PDEV).transpose(1, 0, 2)
    j_vel = pred_vel.reshape(3, N_BLK, N_SUB * PDEV).transpose(1, 0, 2)
    j_mass = mass.reshape(N_BLK, N_SUB * PDEV)

    def one_tile(tile_args):
        tile_pos, tile_vel = tile_args

        def add_block(state_now, j_block):
            accel_part, jerk_part = pair_terms(tile_pos, tile_vel, j_block[0], j_block[1], j_block[2])
            return ((state_now[0] + accel_part, state_now[1] + jerk_part), None)
        zero_init = jnp.zeros((3, LCAP), jnp.float32)
        totals, unused = lax.scan(add_block, (zero_init, zero_init), (j_pos, j_vel, j_mass))
        return totals
    accel_t, jerk_t = lax.map(one_tile, (tiled_pos, tiled_vel))
    new_accel = accel_t.transpose(1, 0, 2).reshape(3, n_rows)
    new_jerk = jerk_t.transpose(1, 0, 2).reshape(3, n_rows)
    new_forces = jnp.concatenate([new_accel, new_jerk], axis=0)
    shaped_forces = new_forces.reshape(6, LEVELS, n_dev * LCAP)
    active_forces = jnp.where(is_live[None, :, :], shaped_forces, jnp.zeros_like(shaped_forces))
    pred_rows = jnp.concatenate([i_pos, i_vel], axis=0)
    corrected = correct(pred_rows, derivs[:, flat_rows], elapsed[flat_rows], new_forces)
    target = jnp.where(is_live.reshape(-1), flat_rows, NSTARS).astype(jnp.int32)
    new_phase = phase.at[:, target].set(corrected, mode='drop')
    new_derivs = derivs.at[:, target].set(new_forces, mode='drop')
    return (new_phase, new_derivs, active_forces)
```

```python
import jax
import jax.numpy as jnp
from jax import lax
from jax.experimental import pallas as pl
from jax.experimental.pallas import tpu as pltpu
from jax.sharding import PartitionSpec as P

LEVELS = 3
LCAP = 64
SUBLANES = 8
LANES = 128

SOFTEN_SQ = 0.0025


def predict(phase, derivs, elapsed):
    t_now = elapsed[None, :]
    pos_pred = (
        phase[:3]
        + t_now * phase[3:]
        + t_now * t_now / 2.0 * derivs[:3]
        + t_now * t_now * t_now / 6.0 * derivs[3:]
    )
    vel_pred = phase[3:] + t_now * derivs[:3] + t_now * t_now / 2.0 * derivs[3:]
    return (pos_pred, vel_pred)


def correct(pred_rows, old_rows, step_len, new_forces):
    diff_acc = old_rows[:3] - new_forces[:3]
    step_row = step_len[None, :]
    term_two = -6.0 * diff_acc - step_row * (4.0 * old_rows[3:] + 2.0 * new_forces[3:])
    term_three = 12.0 * diff_acc + 6.0 * step_row * (old_rows[3:] + new_forces[3:])
    pos_new = pred_rows[:3] + step_row * step_row * (term_two / 24.0 + term_three / 120.0)
    vel_new = pred_rows[3:] + step_row * (term_two / 6.0 + term_three / 24.0)
    return jnp.concatenate([pos_new, vel_new], axis=0)


def pair_sums(row, stars, accs):
    xi, yi, zi, ui, vi, wi = row
    xk, yk, zk, uk, vk, wk, mk = stars
    dx = xk - xi
    dy = yk - yi
    dz = zk - zi
    du = uk - ui
    dv = vk - vi
    dw = wk - wi
    dist_sq = dx * dx + dy * dy + dz * dz + SOFTEN_SQ
    inverse = lax.rsqrt(dist_sq)
    inv_sq = inverse * inverse
    weight = mk * (inv_sq * inverse)
    radial = (weight * inv_sq) * (dx * du + dy * dv + dz * dw)
    ax, ay, az, jx, jy, jz, qx, qy, qz = accs
    return (
        ax + weight * dx,
        ay + weight * dy,
        az + weight * dz,
        jx + weight * du,
        jy + weight * dv,
        jz + weight * dw,
        qx + radial * dx,
        qy + radial * dy,
        qz + radial * dz,
    )


def forces_kernel(counts_ref, rows_ref, stars_ref, out_ref):
    n_rows = out_ref.shape[1]
    n_vregs = stars_ref.shape[1] // SUBLANES
    out_ref[...] = jnp.zeros(out_ref.shape, jnp.float32)
    zero = jnp.zeros((SUBLANES, LANES), jnp.float32)

    def row_scalars(r):
        return tuple(rows_ref[c * n_rows + r] for c in range(6))

    for level in range(LEVELS):
        n_pairs = (counts_ref[level] + 1) // 2

        def pair_body(p, carry, level=level):
            r0 = level * LCAP + 2 * p
            r1 = r0 + 1
            row0 = row_scalars(r0)
            row1 = row_scalars(r1)

            def star_body(j, accs):
                base = pl.multiple_of(j * SUBLANES, SUBLANES)
                stars = tuple(stars_ref[c, pl.ds(base, SUBLANES), :] for c in range(7))
                return pair_sums(row0, stars, accs[:9]) + pair_sums(row1, stars, accs[9:])

            accs = lax.fori_loop(0, n_vregs, star_body, (zero,) * 18, unroll=2)
            for r, part in ((r0, accs[:9]), (r1, accs[9:])):
                ax, ay, az, jx, jy, jz, qx, qy, qz = part
                vals = (ax, ay, az, jx - 3.0 * qx, jy - 3.0 * qy, jz - 3.0 * qz)
                for c in range(6):
                    out_ref[c, pl.ds(r, 1), :] = jnp.sum(vals[c], axis=0, keepdims=True)
            return carry

        lax.fori_loop(0, n_pairs, pair_body, 0)


def own_forces(counts, rows, stars):
    n_rows = rows.shape[1]
    n_stars = stars.shape[1] * LANES
    return pl.pallas_call(
        forces_kernel,
        out_shape=jax.ShapeDtypeStruct((6, n_rows, LANES), jnp.float32),
        in_specs=[
            pl.BlockSpec(memory_space=pltpu.SMEM),
            pl.BlockSpec(memory_space=pltpu.SMEM),
            pl.BlockSpec(memory_space=pltpu.VMEM),
        ],
        out_specs=pl.BlockSpec(memory_space=pltpu.VMEM),
        cost_estimate=pl.CostEstimate(
            flops=40 * n_rows * n_stars,
            transcendentals=n_rows * n_stars,
            bytes_accessed=4 * (stars.size + 6 * n_rows * LANES),
        ),
    )(counts, rows.reshape(-1), stars)


def on_device(phase, derivs, mass, elapsed, active_slots, active_counts):
    pred_pos, pred_vel = predict(phase, derivs, elapsed)
    slot_rows = active_slots.reshape(-1)
    live_grid = lax.broadcasted_iota(jnp.int32, (LEVELS, LCAP), 1) < active_counts
    is_live = live_grid.reshape(-1)
    targets = jnp.concatenate([pred_pos[:, slot_rows], pred_vel[:, slot_rows]], axis=0)

    n_local = phase.shape[1]
    local_stars = jnp.concatenate([pred_pos, pred_vel, mass[None, :]], axis=0)
    local_stars = local_stars.reshape(7, n_local // LANES, LANES)
    all_stars = lax.all_gather(local_stars, ("blk", "sub"), axis=1, tiled=True)

    partial = own_forces(active_counts.reshape(-1), targets, all_stars)
    new_forces = jnp.sum(partial, axis=2)

    shaped_forces = new_forces.reshape(6, LEVELS, LCAP)
    active_forces = jnp.where(live_grid[None, :, :], shaped_forces, jnp.zeros_like(shaped_forces))
    corrected = correct(targets, derivs[:, slot_rows], elapsed[slot_rows], new_forces)
    kept_phase = jnp.where(is_live[None, :], corrected, phase[:, slot_rows])
    kept_derivs = jnp.where(is_live[None, :], new_forces, derivs[:, slot_rows])
    new_phase = phase.at[:, slot_rows].set(kept_phase)
    new_derivs = derivs.at[:, slot_rows].set(kept_derivs)
    return (new_phase, new_derivs, active_forces)


def solution(mesh):
    in_specs = (
        P(None, ("blk", "sub")),
        P(None, ("blk", "sub")),
        P(("blk", "sub")),
        P(("blk", "sub")),
        P(None, ("blk", "sub")),
        P(None, ("blk", "sub")),
    )
    out_specs = (P(None, ("blk", "sub")), P(None, ("blk", "sub")), P(None, None, ("blk", "sub")))
    return jax.shard_map(
        on_device, mesh=mesh, in_specs=in_specs, out_specs=out_specs, check_vma=False
    )
```

```python
import jax
import jax.numpy as jnp
from jax import lax
from jax.experimental import pallas as pl
from jax.experimental.pallas import tpu as pltpu
from jax.sharding import PartitionSpec as P

LEVELS = 3
LCAP = 64
SUBLANES = 8
LANES = 128

SOFTEN_SQ = 0.0025
N_CHUNKS = 2


def predict(phase, derivs, elapsed):
    t_now = elapsed[None, :]
    pos_pred = (
        phase[:3]
        + t_now * phase[3:]
        + t_now * t_now / 2.0 * derivs[:3]
        + t_now * t_now * t_now / 6.0 * derivs[3:]
    )
    vel_pred = phase[3:] + t_now * derivs[:3] + t_now * t_now / 2.0 * derivs[3:]
    return (pos_pred, vel_pred)


def correct(pred_rows, old_rows, step_len, new_forces):
    diff_acc = old_rows[:3] - new_forces[:3]
    step_row = step_len[None, :]
    term_two = -6.0 * diff_acc - step_row * (4.0 * old_rows[3:] + 2.0 * new_forces[3:])
    term_three = 12.0 * diff_acc + 6.0 * step_row * (old_rows[3:] + new_forces[3:])
    pos_new = pred_rows[:3] + step_row * step_row * (term_two / 24.0 + term_three / 120.0)
    vel_new = pred_rows[3:] + step_row * (term_two / 6.0 + term_three / 24.0)
    return jnp.concatenate([pos_new, vel_new], axis=0)


def pair_sums(row, stars, accs):
    xi, yi, zi, ui, vi, wi = row
    xk, yk, zk, uk, vk, wk, mk = stars
    dx = xk - xi
    dy = yk - yi
    dz = zk - zi
    du = uk - ui
    dv = vk - vi
    dw = wk - wi
    dist_sq = dx * dx + dy * dy + dz * dz + SOFTEN_SQ
    inverse = lax.rsqrt(dist_sq)
    inv_sq = inverse * inverse
    weight = mk * (inv_sq * inverse)
    radial = (weight * inv_sq) * (dx * du + dy * dv + dz * dw)
    ax, ay, az, jx, jy, jz, qx, qy, qz = accs
    return (
        ax + weight * dx,
        ay + weight * dy,
        az + weight * dz,
        jx + weight * du,
        jy + weight * dv,
        jz + weight * dw,
        qx + radial * dx,
        qy + radial * dy,
        qz + radial * dz,
    )


def forces_kernel(pairs_ref, rows_ref, stars_ref, acc_ref, out_ref):
    n_rows = out_ref.shape[1]
    n_blocks = pairs_ref.shape[0]
    per_block = n_rows // n_blocks
    n_vregs = stars_ref.shape[1] // SUBLANES
    zero = jnp.zeros((SUBLANES, LANES), jnp.float32)
    out_ref[...] = acc_ref[...]

    def row_scalars(r):
        return tuple(rows_ref[c * n_rows + r] for c in range(6))

    for block in range(n_blocks):

        def pair_body(p, carry, block=block):
            r0 = block * per_block + 2 * p
            r1 = r0 + 1
            row0 = row_scalars(r0)
            row1 = row_scalars(r1)

            def star_body(j, accs):
                base = pl.multiple_of(j * SUBLANES, SUBLANES)
                stars = tuple(stars_ref[c, pl.ds(base, SUBLANES), :] for c in range(7))
                return pair_sums(row0, stars, accs[:9]) + pair_sums(row1, stars, accs[9:])

            accs = lax.fori_loop(0, n_vregs, star_body, (zero,) * 18, unroll=2)
            for r, part in ((r0, accs[:9]), (r1, accs[9:])):
                ax, ay, az, jx, jy, jz, qx, qy, qz = part
                vals = (ax, ay, az, jx - 3.0 * qx, jy - 3.0 * qy, jz - 3.0 * qz)
                for c in range(6):
                    out_ref[c, pl.ds(r, 1), :] = out_ref[c, pl.ds(r, 1), :] + jnp.sum(
                        vals[c], axis=0, keepdims=True
                    )
            return carry

        lax.fori_loop(0, pairs_ref[block], pair_body, 0)


def add_forces(pairs, rows, stars, acc):
    n_rows = rows.shape[1]
    n_stars = stars.shape[1] * LANES
    return pl.pallas_call(
        forces_kernel,
        out_shape=jax.ShapeDtypeStruct(acc.shape, jnp.float32),
        in_specs=[
            pl.BlockSpec(memory_space=pltpu.SMEM),
            pl.BlockSpec(memory_space=pltpu.SMEM),
            pl.BlockSpec(memory_space=pltpu.VMEM),
            pl.BlockSpec(memory_space=pltpu.VMEM),
        ],
        out_specs=pl.BlockSpec(memory_space=pltpu.VMEM),
        input_output_aliases={3: 0},
        cost_estimate=pl.CostEstimate(
            flops=40 * n_rows * n_stars,
            transcendentals=n_rows * n_stars,
            bytes_accessed=4 * (stars.size + 2 * acc.size),
        ),
    )(pairs, rows.reshape(-1), stars, acc)


def on_device(phase, derivs, mass, elapsed, active_slots, active_counts):
    pred_pos, pred_vel = predict(phase, derivs, elapsed)
    slot_rows = active_slots.reshape(-1)
    live_grid = lax.broadcasted_iota(jnp.int32, (LEVELS, LCAP), 1) < active_counts
    is_live = live_grid.reshape(-1)
    targets = jnp.concatenate([pred_pos[:, slot_rows], pred_vel[:, slot_rows]], axis=0)

    n_sub = lax.axis_size("sub")
    me = lax.axis_index("sub")
    group_rows = lax.all_gather(targets, "sub", axis=1, tiled=True)
    group_counts = lax.all_gather(active_counts.reshape(-1), "sub", axis=0, tiled=True)
    n_blocks = group_counts.shape[0]
    per_block = LCAP // n_sub
    dealt = group_rows.reshape(6, n_blocks, per_block, n_sub)
    my_rows = lax.dynamic_slice_in_dim(dealt, me, 1, axis=3).reshape(6, n_blocks * per_block)
    my_counts = jnp.maximum(group_counts - me + n_sub - 1, 0) // n_sub
    my_pairs = (my_counts + 1) // 2

    n_local = phase.shape[1]
    local_stars = jnp.concatenate([pred_pos, pred_vel, mass[None, :]], axis=0)
    local_stars = local_stars.reshape(7, n_local // LANES, LANES)
    n_chunks = N_CHUNKS
    rows_per_chunk = local_stars.shape[1] // n_chunks
    acc = jnp.zeros((6, n_blocks * per_block, LANES), jnp.float32)
    for chunk in range(n_chunks):
        piece = local_stars[:, chunk * rows_per_chunk:(chunk + 1) * rows_per_chunk, :]
        stars = lax.all_gather(piece, ("blk", "sub"), axis=1, tiled=True)
        acc = add_forces(my_pairs, my_rows, stars, acc)
    my_forces = jnp.sum(acc, axis=2).reshape(6, n_blocks, per_block, 1)

    placed = jnp.where(
        lax.broadcasted_iota(jnp.int32, (1, 1, 1, n_sub), 3) == me, my_forces, 0.0
    ).reshape(6, n_blocks * LCAP)
    new_forces = lax.psum_scatter(placed, "sub", scatter_dimension=1, tiled=True)

    shaped_forces = new_forces.reshape(6, LEVELS, LCAP)
    active_forces = jnp.where(live_grid[None, :, :], shaped_forces, jnp.zeros_like(shaped_forces))
    corrected = correct(targets, derivs[:, slot_rows], elapsed[slot_rows], new_forces)
    kept_phase = jnp.where(is_live[None, :], corrected, phase[:, slot_rows])
    kept_derivs = jnp.where(is_live[None, :], new_forces, derivs[:, slot_rows])
    new_phase = phase.at[:, slot_rows].set(kept_phase)
    new_derivs = derivs.at[:, slot_rows].set(kept_derivs)
    return (new_phase, new_derivs, active_forces)


def solution(mesh):
    in_specs = (
        P(None, ("blk", "sub")),
        P(None, ("blk", "sub")),
        P(("blk", "sub")),
        P(("blk", "sub")),
        P(None, ("blk", "sub")),
        P(None, ("blk", "sub")),
    )
    out_specs = (P(None, ("blk", "sub")), P(None, ("blk", "sub")), P(None, None, ("blk", "sub")))
    return jax.shard_map(
        on_device, mesh=mesh, in_specs=in_specs, out_specs=out_specs, check_vma=False
    )
```

```python
import jax
import jax.numpy as jnp
from jax import lax
from jax.experimental import pallas as pl
from jax.experimental.pallas import tpu as pltpu
from jax.sharding import PartitionSpec as P

LEVELS = 3
LCAP = 64
SUBLANES = 8
LANES = 128

SOFTEN_SQ = 0.0025
N_CHUNKS = 2
ROWS_PER_TRIP = 1
UNROLL = 8


def predict(phase, derivs, elapsed):
    t_now = elapsed[None, :]
    pos_pred = (
        phase[:3]
        + t_now * phase[3:]
        + t_now * t_now / 2.0 * derivs[:3]
        + t_now * t_now * t_now / 6.0 * derivs[3:]
    )
    vel_pred = phase[3:] + t_now * derivs[:3] + t_now * t_now / 2.0 * derivs[3:]
    return (pos_pred, vel_pred)


def correct(pred_rows, old_rows, step_len, new_forces):
    diff_acc = old_rows[:3] - new_forces[:3]
    step_row = step_len[None, :]
    term_two = -6.0 * diff_acc - step_row * (4.0 * old_rows[3:] + 2.0 * new_forces[3:])
    term_three = 12.0 * diff_acc + 6.0 * step_row * (old_rows[3:] + new_forces[3:])
    pos_new = pred_rows[:3] + step_row * step_row * (term_two / 24.0 + term_three / 120.0)
    vel_new = pred_rows[3:] + step_row * (term_two / 6.0 + term_three / 24.0)
    return jnp.concatenate([pos_new, vel_new], axis=0)


def pair_sums(row, stars, accs):
    xi, yi, zi, ui, vi, wi = row
    xk, yk, zk, uk, vk, wk, mk = stars
    dx = xk - xi
    dy = yk - yi
    dz = zk - zi
    du = uk - ui
    dv = vk - vi
    dw = wk - wi
    dist_sq = dx * dx + dy * dy + dz * dz + SOFTEN_SQ
    inverse = lax.rsqrt(dist_sq)
    inv_sq = inverse * inverse
    weight = mk * (inv_sq * inverse)
    radial = (weight * inv_sq) * (dx * du + dy * dv + dz * dw)
    ax, ay, az, jx, jy, jz, qx, qy, qz = accs
    return (
        ax + weight * dx,
        ay + weight * dy,
        az + weight * dz,
        jx + weight * du,
        jy + weight * dv,
        jz + weight * dw,
        qx + radial * dx,
        qy + radial * dy,
        qz + radial * dz,
    )


def forces_kernel(trips_ref, rows_ref, stars_ref, acc_ref, out_ref):
    n_rows = out_ref.shape[1]
    n_blocks = trips_ref.shape[0]
    per_block = n_rows // n_blocks
    n_vregs = stars_ref.shape[1] // SUBLANES
    zero = jnp.zeros((SUBLANES, LANES), jnp.float32)
    out_ref[...] = acc_ref[...]

    def row_vectors(r):
        return tuple(jnp.full((SUBLANES, LANES), rows_ref[c * n_rows + r], jnp.float32) for c in range(6))

    for block in range(n_blocks):

        def trip_body(p, carry, block=block):
            first = block * per_block + ROWS_PER_TRIP * p
            rows = [row_vectors(first + k) for k in range(ROWS_PER_TRIP)]

            def star_body(j, accs):
                base = pl.multiple_of(j * SUBLANES, SUBLANES)
                stars = tuple(stars_ref[c, pl.ds(base, SUBLANES), :] for c in range(7))
                new = ()
                for k in range(ROWS_PER_TRIP):
                    new = new + pair_sums(rows[k], stars, accs[9 * k:9 * k + 9])
                return new

            accs = lax.fori_loop(0, n_vregs, star_body, (zero,) * (9 * ROWS_PER_TRIP), unroll=UNROLL)
            for k in range(ROWS_PER_TRIP):
                ax, ay, az, jx, jy, jz, qx, qy, qz = accs[9 * k:9 * k + 9]
                vals = (ax, ay, az, jx - 3.0 * qx, jy - 3.0 * qy, jz - 3.0 * qz)
                for c in range(6):
                    out_ref[c, pl.ds(first + k, 1), :] = out_ref[c, pl.ds(first + k, 1), :] + jnp.sum(
                        vals[c], axis=0, keepdims=True
                    )
            return carry

        lax.fori_loop(0, trips_ref[block], trip_body, 0)


def add_forces(pairs, rows, stars, acc):
    n_rows = rows.shape[1]
    n_stars = stars.shape[1] * LANES
    return pl.pallas_call(
        forces_kernel,
        out_shape=jax.ShapeDtypeStruct(acc.shape, jnp.float32),
        in_specs=[
            pl.BlockSpec(memory_space=pltpu.SMEM),
            pl.BlockSpec(memory_space=pltpu.SMEM),
            pl.BlockSpec(memory_space=pltpu.VMEM),
            pl.BlockSpec(memory_space=pltpu.VMEM),
        ],
        out_specs=pl.BlockSpec(memory_space=pltpu.VMEM),
        input_output_aliases={3: 0},
        cost_estimate=pl.CostEstimate(
            flops=40 * n_rows * n_stars,
            transcendentals=n_rows * n_stars,
            bytes_accessed=4 * (stars.size + 2 * acc.size),
        ),
    )(pairs, rows.reshape(-1), stars, acc)


def on_device(phase, derivs, mass, elapsed, active_slots, active_counts):
    pred_pos, pred_vel = predict(phase, derivs, elapsed)
    slot_rows = active_slots.reshape(-1)
    live_grid = lax.broadcasted_iota(jnp.int32, (LEVELS, LCAP), 1) < active_counts
    is_live = live_grid.reshape(-1)
    targets = jnp.concatenate([pred_pos[:, slot_rows], pred_vel[:, slot_rows]], axis=0)

    n_sub = lax.axis_size("sub")
    me = lax.axis_index("sub")
    group_rows = lax.all_gather(targets, "sub", axis=1, tiled=True)
    group_counts = lax.all_gather(active_counts.reshape(-1), "sub", axis=0, tiled=True)
    n_blocks = group_counts.shape[0]
    per_block = LCAP // n_sub
    dealt = group_rows.reshape(6, n_blocks, per_block, n_sub)
    my_rows = lax.dynamic_slice_in_dim(dealt, me, 1, axis=3).reshape(6, n_blocks * per_block)
    my_counts = jnp.maximum(group_counts - me + n_sub - 1, 0) // n_sub
    my_trips = (my_counts + ROWS_PER_TRIP - 1) // ROWS_PER_TRIP

    n_local = phase.shape[1]
    local_stars = jnp.concatenate([pred_pos, pred_vel, mass[None, :]], axis=0)
    local_stars = local_stars.reshape(7, n_local // LANES, LANES)
    n_chunks = N_CHUNKS
    rows_per_chunk = local_stars.shape[1] // n_chunks
    acc = jnp.zeros((6, n_blocks * per_block, LANES), jnp.float32)
    for chunk in range(n_chunks):
        piece = local_stars[:, chunk * rows_per_chunk:(chunk + 1) * rows_per_chunk, :]
        stars = lax.all_gather(piece, ("blk", "sub"), axis=1, tiled=True)
        acc = add_forces(my_trips, my_rows, stars, acc)
    my_forces = jnp.sum(acc, axis=2).reshape(6, n_blocks, per_block, 1)

    placed = jnp.where(
        lax.broadcasted_iota(jnp.int32, (1, 1, 1, n_sub), 3) == me, my_forces, 0.0
    ).reshape(6, n_blocks * LCAP)
    new_forces = lax.psum_scatter(placed, "sub", scatter_dimension=1, tiled=True)

    shaped_forces = new_forces.reshape(6, LEVELS, LCAP)
    active_forces = jnp.where(live_grid[None, :, :], shaped_forces, jnp.zeros_like(shaped_forces))
    corrected = correct(targets, derivs[:, slot_rows], elapsed[slot_rows], new_forces)
    kept_phase = jnp.where(is_live[None, :], corrected, phase[:, slot_rows])
    kept_derivs = jnp.where(is_live[None, :], new_forces, derivs[:, slot_rows])
    new_phase = phase.at[:, slot_rows].set(kept_phase)
    new_derivs = derivs.at[:, slot_rows].set(kept_derivs)
    return (new_phase, new_derivs, active_forces)


def solution(mesh):
    in_specs = (
        P(None, ("blk", "sub")),
        P(None, ("blk", "sub")),
        P(("blk", "sub")),
        P(("blk", "sub")),
        P(None, ("blk", "sub")),
        P(None, ("blk", "sub")),
    )
    out_specs = (P(None, ("blk", "sub")), P(None, ("blk", "sub")), P(None, None, ("blk", "sub")))
    return jax.shard_map(
        on_device, mesh=mesh, in_specs=in_specs, out_specs=out_specs, check_vma=False
    )
```

```python
import jax
import jax.numpy as jnp
from jax import lax
from jax.experimental import pallas as pl
from jax.experimental.pallas import tpu as pltpu
from jax.sharding import PartitionSpec as P

LEVELS = 3
LCAP = 64
SUBLANES = 8
LANES = 128

SOFTEN_SQ = 0.0025
MIN_ROWS = 64
VPU_COST = 5000
ROWS_PER_TRIP = 1
UNROLL = 8


def predict(phase, derivs, elapsed):
    t_now = elapsed[None, :]
    pos_pred = (
        phase[:3]
        + t_now * phase[3:]
        + t_now * t_now / 2.0 * derivs[:3]
        + t_now * t_now * t_now / 6.0 * derivs[3:]
    )
    vel_pred = phase[3:] + t_now * derivs[:3] + t_now * t_now / 2.0 * derivs[3:]
    return (pos_pred, vel_pred)


def correct(pred_rows, old_rows, step_len, new_forces):
    diff_acc = old_rows[:3] - new_forces[:3]
    step_row = step_len[None, :]
    term_two = -6.0 * diff_acc - step_row * (4.0 * old_rows[3:] + 2.0 * new_forces[3:])
    term_three = 12.0 * diff_acc + 6.0 * step_row * (old_rows[3:] + new_forces[3:])
    pos_new = pred_rows[:3] + step_row * step_row * (term_two / 24.0 + term_three / 120.0)
    vel_new = pred_rows[3:] + step_row * (term_two / 6.0 + term_three / 24.0)
    return jnp.concatenate([pos_new, vel_new], axis=0)


def pair_sums(row, stars, accs):
    xi, yi, zi, ui, vi, wi = row
    xk, yk, zk, uk, vk, wk, mk = stars
    dx = xk - xi
    dy = yk - yi
    dz = zk - zi
    du = uk - ui
    dv = vk - vi
    dw = wk - wi
    dist_sq = dx * dx + dy * dy + dz * dz + SOFTEN_SQ
    inverse = lax.rsqrt(dist_sq)
    inv_sq = inverse * inverse
    weight = mk * (inv_sq * inverse)
    radial = (weight * inv_sq) * (dx * du + dy * dv + dz * dw)
    ax, ay, az, jx, jy, jz, qx, qy, qz = accs
    return (
        ax + weight * dx,
        ay + weight * dy,
        az + weight * dz,
        jx + weight * du,
        jy + weight * dv,
        jz + weight * dw,
        qx + radial * dx,
        qy + radial * dy,
        qz + radial * dz,
    )


def forces_kernel(trips_ref, rows_ref, stars_ref, acc_ref, out_ref):
    n_rows = out_ref.shape[1]
    n_blocks = trips_ref.shape[0]
    per_block = n_rows // n_blocks
    n_vregs = stars_ref.shape[1] // SUBLANES
    zero = jnp.zeros((SUBLANES, LANES), jnp.float32)
    out_ref[...] = acc_ref[...]

    def row_vectors(r):
        return tuple(jnp.full((SUBLANES, LANES), rows_ref[c * n_rows + r], jnp.float32) for c in range(6))

    for block in range(n_blocks):

        def trip_body(p, carry, block=block):
            first = block * per_block + ROWS_PER_TRIP * p
            rows = [row_vectors(first + k) for k in range(ROWS_PER_TRIP)]

            def star_body(j, accs):
                base = pl.multiple_of(j * SUBLANES, SUBLANES)
                stars = tuple(stars_ref[c, pl.ds(base, SUBLANES), :] for c in range(7))
                new = ()
                for k in range(ROWS_PER_TRIP):
                    new = new + pair_sums(rows[k], stars, accs[9 * k:9 * k + 9])
                return new

            accs = lax.fori_loop(0, n_vregs, star_body, (zero,) * (9 * ROWS_PER_TRIP), unroll=UNROLL)
            for k in range(ROWS_PER_TRIP):
                ax, ay, az, jx, jy, jz, qx, qy, qz = accs[9 * k:9 * k + 9]
                vals = (ax, ay, az, jx - 3.0 * qx, jy - 3.0 * qy, jz - 3.0 * qz)
                for c in range(6):
                    out_ref[c, pl.ds(first + k, 1), :] = out_ref[c, pl.ds(first + k, 1), :] + jnp.sum(
                        vals[c], axis=0, keepdims=True
                    )
            return carry

        lax.fori_loop(0, trips_ref[block], trip_body, 0)


def add_forces(pairs, rows, stars, acc):
    n_rows = rows.shape[1]
    n_stars = stars.shape[1] * LANES
    return pl.pallas_call(
        forces_kernel,
        out_shape=jax.ShapeDtypeStruct(acc.shape, jnp.float32),
        in_specs=[
            pl.BlockSpec(memory_space=pltpu.SMEM),
            pl.BlockSpec(memory_space=pltpu.SMEM),
            pl.BlockSpec(memory_space=pltpu.VMEM),
            pl.BlockSpec(memory_space=pltpu.VMEM),
        ],
        out_specs=pl.BlockSpec(memory_space=pltpu.VMEM),
        input_output_aliases={3: 0},
        cost_estimate=pl.CostEstimate(
            flops=VPU_COST * n_rows * n_stars,
            transcendentals=n_rows * n_stars,
            bytes_accessed=4 * (stars.size + 2 * acc.size),
        ),
    )(pairs, rows.reshape(-1), stars, acc)


def xor_swap(x, axis, bit):
    n = lax.axis_size(axis)
    return lax.ppermute(x, axis, [(i, i ^ bit) for i in range(n)])


def in_order(mine, theirs, upper):
    return jnp.where(upper, jnp.concatenate([theirs, mine], axis=1), jnp.concatenate([mine, theirs], axis=1))


def on_device(phase, derivs, mass, elapsed, active_slots, active_counts):
    pred_pos, pred_vel = predict(phase, derivs, elapsed)
    slot_rows = active_slots.reshape(-1)
    live_grid = lax.broadcasted_iota(jnp.int32, (LEVELS, LCAP), 1) < active_counts
    is_live = live_grid.reshape(-1)
    targets = jnp.concatenate([pred_pos[:, slot_rows], pred_vel[:, slot_rows]], axis=0)
    n_slots = targets.shape[1]

    n_sub = lax.axis_size("sub")
    me = lax.axis_index("sub")
    count_row = jnp.zeros((1, n_slots), jnp.float32).at[0, :LEVELS].set(
        active_counts.reshape(-1).astype(jnp.float32)
    )
    group = jnp.concatenate([targets, count_row], axis=0)
    bit = 1
    while bit < n_sub:
        group = in_order(group, xor_swap(group, "sub", bit), (me & bit) != 0)
        bit *= 2
    group_rows = group[:6]
    group_counts = group[6].reshape(n_sub, n_slots)[:, :LEVELS].reshape(-1).astype(jnp.int32)

    n_blocks = group_counts.shape[0]
    per_block = LCAP // n_sub
    offsets = (me - jnp.arange(n_blocks, dtype=jnp.int32)) % n_sub
    dealt = group_rows.reshape(6, n_blocks, per_block, n_sub)
    my_rows = jnp.take_along_axis(dealt, offsets.reshape(1, n_blocks, 1, 1), axis=3)
    my_rows = my_rows.reshape(6, n_blocks * per_block)
    my_counts = jnp.maximum(group_counts - offsets + n_sub - 1, 0) // n_sub
    my_trips = (my_counts + ROWS_PER_TRIP - 1) // ROWS_PER_TRIP

    n_local = phase.shape[1]
    have = jnp.concatenate([pred_pos, pred_vel, mass[None, :]], axis=0)
    have = have.reshape(7, n_local // LANES, LANES)
    my_rows, my_trips, have = lax.optimization_barrier((my_rows, my_trips, have))
    acc = jnp.zeros((6, n_blocks * per_block, LANES), jnp.float32)
    stages = []
    bit = 1
    while bit < lax.axis_size("blk"):
        stages.append(("blk", bit))
        bit *= 2
    bit = n_sub // 2
    while bit >= 1:
        stages.append(("sub", bit))
        bit //= 2
    pending = None
    for axis, bit in stages:
        theirs = xor_swap(have, axis, bit)
        if pending is None and have.shape[1] + theirs.shape[1] >= MIN_ROWS:
            pending = jnp.concatenate([have, theirs], axis=1)
        elif pending is not None:
            pending = theirs
        if pending is not None:
            acc = add_forces(my_trips, my_rows, pending, acc)
        have = jnp.concatenate([have, theirs], axis=1)
    my_forces = jnp.sum(acc, axis=2).reshape(6, n_blocks, per_block, 1)

    lane = lax.broadcasted_iota(jnp.int32, (1, n_blocks, 1, n_sub), 3)
    placed = jnp.where(lane == offsets.reshape(1, n_blocks, 1, 1), my_forces, 0.0)
    placed = placed.reshape(6, n_sub, n_slots)
    new_forces = lax.dynamic_index_in_dim(placed, me, axis=1, keepdims=False)
    for step in range(1, n_sub):
        outgoing = lax.dynamic_index_in_dim(placed, me ^ step, axis=1, keepdims=False)
        new_forces = new_forces + xor_swap(outgoing, "sub", step)

    shaped_forces = new_forces.reshape(6, LEVELS, LCAP)
    active_forces = jnp.where(live_grid[None, :, :], shaped_forces, jnp.zeros_like(shaped_forces))
    corrected = correct(targets, derivs[:, slot_rows], elapsed[slot_rows], new_forces)
    kept_phase = jnp.where(is_live[None, :], corrected, phase[:, slot_rows])
    kept_derivs = jnp.where(is_live[None, :], new_forces, derivs[:, slot_rows])
    new_phase = phase.at[:, slot_rows].set(kept_phase)
    new_derivs = derivs.at[:, slot_rows].set(kept_derivs)
    return (new_phase, new_derivs, active_forces)


def solution(mesh):
    in_specs = (
        P(None, ("blk", "sub")),
        P(None, ("blk", "sub")),
        P(("blk", "sub")),
        P(("blk", "sub")),
        P(None, ("blk", "sub")),
        P(None, ("blk", "sub")),
    )
    out_specs = (P(None, ("blk", "sub")), P(None, ("blk", "sub")), P(None, None, ("blk", "sub")))
    return jax.shard_map(
        on_device, mesh=mesh, in_specs=in_specs, out_specs=out_specs, check_vma=False
    )
```

```python
import jax
import jax.numpy as jnp
from jax import lax
from jax.experimental import pallas as pl
from jax.experimental.pallas import tpu as pltpu
from jax.sharding import PartitionSpec as P

LEVELS = 3
LCAP = 64
SUBLANES = 8
LANES = 128

SOFTEN_SQ = 0.0025
MIN_ROWS = 64
VPU_COST = 5000
ROWS_PER_TRIP = 1
UNROLL = 8


def predict(phase, derivs, elapsed):
    t_now = elapsed[None, :]
    pos_pred = (
        phase[:3]
        + t_now * phase[3:]
        + t_now * t_now / 2.0 * derivs[:3]
        + t_now * t_now * t_now / 6.0 * derivs[3:]
    )
    vel_pred = phase[3:] + t_now * derivs[:3] + t_now * t_now / 2.0 * derivs[3:]
    return (pos_pred, vel_pred)


def correct(pred_rows, old_rows, step_len, new_forces):
    diff_acc = old_rows[:3] - new_forces[:3]
    step_row = step_len[None, :]
    term_two = -6.0 * diff_acc - step_row * (4.0 * old_rows[3:] + 2.0 * new_forces[3:])
    term_three = 12.0 * diff_acc + 6.0 * step_row * (old_rows[3:] + new_forces[3:])
    pos_new = pred_rows[:3] + step_row * step_row * (term_two / 24.0 + term_three / 120.0)
    vel_new = pred_rows[3:] + step_row * (term_two / 6.0 + term_three / 24.0)
    return jnp.concatenate([pos_new, vel_new], axis=0)


def pair_sums(row, stars, accs):
    xi, yi, zi, ui, vi, wi = row
    xk, yk, zk, uk, vk, wk, mk = stars
    dx = xk - xi
    dy = yk - yi
    dz = zk - zi
    du = uk - ui
    dv = vk - vi
    dw = wk - wi
    dist_sq = dx * dx + dy * dy + dz * dz + SOFTEN_SQ
    inverse = lax.rsqrt(dist_sq)
    inv_sq = inverse * inverse
    weight = mk * (inv_sq * inverse)
    radial = (weight * inv_sq) * (dx * du + dy * dv + dz * dw)
    ax, ay, az, jx, jy, jz, qx, qy, qz = accs
    return (
        ax + weight * dx,
        ay + weight * dy,
        az + weight * dz,
        jx + weight * du,
        jy + weight * dv,
        jz + weight * dw,
        qx + radial * dx,
        qy + radial * dy,
        qz + radial * dz,
    )


def forces_kernel(trips_ref, rows_ref, stars_ref, acc_ref, out_ref):
    n_rows = out_ref.shape[1]
    n_blocks = trips_ref.shape[0]
    per_block = n_rows // n_blocks
    n_vregs = stars_ref.shape[1] // SUBLANES
    zero = jnp.zeros((SUBLANES, LANES), jnp.float32)
    out_ref[...] = acc_ref[...]

    def row_vectors(r):
        return tuple(rows_ref[c * n_rows + r] for c in range(6))

    for block in range(n_blocks):

        def trip_body(p, carry, block=block):
            first = block * per_block + ROWS_PER_TRIP * p
            rows = [row_vectors(first + k) for k in range(ROWS_PER_TRIP)]

            def star_body(j, accs):
                base = pl.multiple_of(j * SUBLANES, SUBLANES)
                stars = tuple(stars_ref[c, pl.ds(base, SUBLANES), :] for c in range(7))
                new = ()
                for k in range(ROWS_PER_TRIP):
                    new = new + pair_sums(rows[k], stars, accs[9 * k:9 * k + 9])
                return new

            accs = lax.fori_loop(0, n_vregs, star_body, (zero,) * (9 * ROWS_PER_TRIP), unroll=UNROLL)
            for k in range(ROWS_PER_TRIP):
                ax, ay, az, jx, jy, jz, qx, qy, qz = accs[9 * k:9 * k + 9]
                vals = (ax, ay, az, jx - 3.0 * qx, jy - 3.0 * qy, jz - 3.0 * qz)
                for c in range(6):
                    out_ref[c, pl.ds(first + k, 1), :] = out_ref[c, pl.ds(first + k, 1), :] + jnp.sum(
                        vals[c], axis=0, keepdims=True
                    )
            return carry

        lax.fori_loop(0, trips_ref[block], trip_body, 0)


def add_forces(pairs, rows, stars, acc):
    n_rows = rows.shape[1]
    n_stars = stars.shape[1] * LANES
    return pl.pallas_call(
        forces_kernel,
        out_shape=jax.ShapeDtypeStruct(acc.shape, jnp.float32),
        in_specs=[
            pl.BlockSpec(memory_space=pltpu.SMEM),
            pl.BlockSpec(memory_space=pltpu.SMEM),
            pl.BlockSpec(memory_space=pltpu.VMEM),
            pl.BlockSpec(memory_space=pltpu.VMEM),
        ],
        out_specs=pl.BlockSpec(memory_space=pltpu.VMEM),
        input_output_aliases={3: 0},
        cost_estimate=pl.CostEstimate(
            flops=VPU_COST * n_rows * n_stars,
            transcendentals=n_rows * n_stars,
            bytes_accessed=4 * (stars.size + 2 * acc.size),
        ),
    )(pairs, rows.reshape(-1), stars, acc)


def xor_swap(x, axis, bit):
    n = lax.axis_size(axis)
    return lax.ppermute(x, axis, [(i, i ^ bit) for i in range(n)])


def in_order(mine, theirs, upper):
    return jnp.where(upper, jnp.concatenate([theirs, mine], axis=1), jnp.concatenate([mine, theirs], axis=1))


def on_device(phase, derivs, mass, elapsed, active_slots, active_counts):
    pred_pos, pred_vel = predict(phase, derivs, elapsed)
    slot_rows = active_slots.reshape(-1)
    live_grid = lax.broadcasted_iota(jnp.int32, (LEVELS, LCAP), 1) < active_counts
    is_live = live_grid.reshape(-1)
    targets = jnp.concatenate([pred_pos[:, slot_rows], pred_vel[:, slot_rows]], axis=0)
    n_slots = targets.shape[1]

    n_sub = lax.axis_size("sub")
    me = lax.axis_index("sub")
    count_row = jnp.zeros((1, n_slots), jnp.float32).at[0, :LEVELS].set(
        active_counts.reshape(-1).astype(jnp.float32)
    )
    group = jnp.concatenate([targets, count_row], axis=0)
    bit = 1
    while bit < n_sub:
        group = in_order(group, xor_swap(group, "sub", bit), (me & bit) != 0)
        bit *= 2
    group_rows = group[:6]
    group_counts = group[6].reshape(n_sub, n_slots)[:, :LEVELS].reshape(-1).astype(jnp.int32)

    n_blocks = group_counts.shape[0]
    per_block = LCAP // n_sub
    offsets = (me - jnp.arange(n_blocks, dtype=jnp.int32)) % n_sub
    dealt = group_rows.reshape(6, n_blocks, per_block, n_sub)
    my_rows = jnp.take_along_axis(dealt, offsets.reshape(1, n_blocks, 1, 1), axis=3)
    my_rows = my_rows.reshape(6, n_blocks * per_block)
    my_counts = jnp.maximum(group_counts - offsets + n_sub - 1, 0) // n_sub
    my_trips = (my_counts + ROWS_PER_TRIP - 1) // ROWS_PER_TRIP

    n_local = phase.shape[1]
    have = jnp.concatenate([pred_pos, pred_vel, mass[None, :]], axis=0)
    have = have.reshape(7, n_local // LANES, LANES)
    acc = jnp.zeros((6, n_blocks * per_block, LANES), jnp.float32)
    stages = []
    bit = 1
    while bit < lax.axis_size("blk"):
        stages.append(("blk", bit))
        bit *= 2
    bit = n_sub // 2
    while bit >= 1:
        stages.append(("sub", bit))
        bit //= 2
    pending = None
    for axis, bit in stages:
        theirs = xor_swap(have, axis, bit)
        if pending is None and have.shape[1] + theirs.shape[1] >= MIN_ROWS:
            pending = jnp.concatenate([have, theirs], axis=1)
        elif pending is not None:
            pending = theirs
        if pending is not None:
            acc = add_forces(my_trips, my_rows, pending, acc)
        have = jnp.concatenate([have, theirs], axis=1)
    my_forces = jnp.sum(acc, axis=2).reshape(6, n_blocks, per_block, 1)

    lane = lax.broadcasted_iota(jnp.int32, (1, n_blocks, 1, n_sub), 3)
    placed = jnp.where(lane == offsets.reshape(1, n_blocks, 1, 1), my_forces, 0.0)
    placed = placed.reshape(6, n_sub, n_slots)
    new_forces = lax.dynamic_index_in_dim(placed, me, axis=1, keepdims=False)
    for step in range(1, n_sub):
        outgoing = lax.dynamic_index_in_dim(placed, me ^ step, axis=1, keepdims=False)
        new_forces = new_forces + xor_swap(outgoing, "sub", step)

    shaped_forces = new_forces.reshape(6, LEVELS, LCAP)
    active_forces = jnp.where(live_grid[None, :, :], shaped_forces, jnp.zeros_like(shaped_forces))
    corrected = correct(targets, derivs[:, slot_rows], elapsed[slot_rows], new_forces)
    kept_phase = jnp.where(is_live[None, :], corrected, phase[:, slot_rows])
    kept_derivs = jnp.where(is_live[None, :], new_forces, derivs[:, slot_rows])
    new_phase = phase.at[:, slot_rows].set(kept_phase)
    new_derivs = derivs.at[:, slot_rows].set(kept_derivs)
    return (new_phase, new_derivs, active_forces)


def solution(mesh):
    in_specs = (
        P(None, ("blk", "sub")),
        P(None, ("blk", "sub")),
        P(("blk", "sub")),
        P(("blk", "sub")),
        P(None, ("blk", "sub")),
        P(None, ("blk", "sub")),
    )
    out_specs = (P(None, ("blk", "sub")), P(None, ("blk", "sub")), P(None, None, ("blk", "sub")))
    return jax.shard_map(
        on_device, mesh=mesh, in_specs=in_specs, out_specs=out_specs, check_vma=False
    )
```

```python
import jax
import jax.numpy as jnp
from jax import lax
from jax.experimental import pallas as pl
from jax.experimental.pallas import tpu as pltpu
from jax.sharding import PartitionSpec as P

LEVELS = 3
LCAP = 64
SUBLANES = 8
LANES = 128

SOFTEN_SQ = 0.0025
WAIT_AFTER = (1,)
VPU_COST = 5000
ROWS_PER_TRIP = 1
UNROLL = 8


def predict(phase, derivs, elapsed):
    t_now = elapsed[None, :]
    pos_pred = (
        phase[:3]
        + t_now * phase[3:]
        + t_now * t_now / 2.0 * derivs[:3]
        + t_now * t_now * t_now / 6.0 * derivs[3:]
    )
    vel_pred = phase[3:] + t_now * derivs[:3] + t_now * t_now / 2.0 * derivs[3:]
    return (pos_pred, vel_pred)


def correct(pred_rows, old_rows, step_len, new_forces):
    diff_acc = old_rows[:3] - new_forces[:3]
    step_row = step_len[None, :]
    term_two = -6.0 * diff_acc - step_row * (4.0 * old_rows[3:] + 2.0 * new_forces[3:])
    term_three = 12.0 * diff_acc + 6.0 * step_row * (old_rows[3:] + new_forces[3:])
    pos_new = pred_rows[:3] + step_row * step_row * (term_two / 24.0 + term_three / 120.0)
    vel_new = pred_rows[3:] + step_row * (term_two / 6.0 + term_three / 24.0)
    return jnp.concatenate([pos_new, vel_new], axis=0)


def pair_sums(row, stars, accs):
    xi, yi, zi, ui, vi, wi = row
    xk, yk, zk, uk, vk, wk, mk = stars
    dx = xk - xi
    dy = yk - yi
    dz = zk - zi
    du = uk - ui
    dv = vk - vi
    dw = wk - wi
    dist_sq = dx * dx + dy * dy + dz * dz + SOFTEN_SQ
    inverse = lax.rsqrt(dist_sq)
    inv_sq = inverse * inverse
    weight = mk * (inv_sq * inverse)
    radial = (weight * inv_sq) * (dx * du + dy * dv + dz * dw)
    ax, ay, az, jx, jy, jz, qx, qy, qz = accs
    return (
        ax + weight * dx,
        ay + weight * dy,
        az + weight * dz,
        jx + weight * du,
        jy + weight * dv,
        jz + weight * dw,
        qx + radial * dx,
        qy + radial * dy,
        qz + radial * dz,
    )


def forces_kernel(trips_ref, rows_ref, stars_ref, acc_ref, out_ref):
    n_rows = out_ref.shape[1]
    n_blocks = trips_ref.shape[0]
    per_block = n_rows // n_blocks
    n_vregs = stars_ref.shape[1] // SUBLANES
    zero = jnp.zeros((SUBLANES, LANES), jnp.float32)
    out_ref[...] = acc_ref[...]

    def row_vectors(r):
        return tuple(rows_ref[c * n_rows + r] for c in range(6))

    for block in range(n_blocks):

        def trip_body(p, carry, block=block):
            first = block * per_block + ROWS_PER_TRIP * p
            rows = [row_vectors(first + k) for k in range(ROWS_PER_TRIP)]

            def star_body(j, accs):
                base = pl.multiple_of(j * SUBLANES, SUBLANES)
                stars = tuple(stars_ref[c, pl.ds(base, SUBLANES), :] for c in range(7))
                new = ()
                for k in range(ROWS_PER_TRIP):
                    new = new + pair_sums(rows[k], stars, accs[9 * k:9 * k + 9])
                return new

            accs = lax.fori_loop(0, n_vregs, star_body, (zero,) * (9 * ROWS_PER_TRIP), unroll=UNROLL)
            for k in range(ROWS_PER_TRIP):
                ax, ay, az, jx, jy, jz, qx, qy, qz = accs[9 * k:9 * k + 9]
                vals = (ax, ay, az, jx - 3.0 * qx, jy - 3.0 * qy, jz - 3.0 * qz)
                for c in range(6):
                    out_ref[c, pl.ds(first + k, 1), :] = out_ref[c, pl.ds(first + k, 1), :] + jnp.sum(
                        vals[c], axis=0, keepdims=True
                    )
            return carry

        lax.fori_loop(0, trips_ref[block], trip_body, 0)


def add_forces(pairs, rows, stars, acc):
    n_rows = rows.shape[1]
    n_stars = stars.shape[1] * LANES
    return pl.pallas_call(
        forces_kernel,
        out_shape=jax.ShapeDtypeStruct(acc.shape, jnp.float32),
        in_specs=[
            pl.BlockSpec(memory_space=pltpu.SMEM),
            pl.BlockSpec(memory_space=pltpu.SMEM),
            pl.BlockSpec(memory_space=pltpu.VMEM),
            pl.BlockSpec(memory_space=pltpu.VMEM),
        ],
        out_specs=pl.BlockSpec(memory_space=pltpu.VMEM),
        input_output_aliases={3: 0},
        cost_estimate=pl.CostEstimate(
            flops=VPU_COST * n_rows * n_stars,
            transcendentals=n_rows * n_stars,
            bytes_accessed=4 * (stars.size + 2 * acc.size),
        ),
    )(pairs, rows.reshape(-1), stars, acc)


def xor_swap(x, axis, bit):
    n = lax.axis_size(axis)
    return lax.ppermute(x, axis, [(i, i ^ bit) for i in range(n)])


def in_order(mine, theirs, upper):
    return jnp.where(upper, jnp.concatenate([theirs, mine], axis=1), jnp.concatenate([mine, theirs], axis=1))


def on_device(phase, derivs, mass, elapsed, active_slots, active_counts):
    pred_pos, pred_vel = predict(phase, derivs, elapsed)
    slot_rows = active_slots.reshape(-1)
    live_grid = lax.broadcasted_iota(jnp.int32, (LEVELS, LCAP), 1) < active_counts
    is_live = live_grid.reshape(-1)
    targets = jnp.concatenate([pred_pos[:, slot_rows], pred_vel[:, slot_rows]], axis=0)
    n_slots = targets.shape[1]

    n_sub = lax.axis_size("sub")
    me = lax.axis_index("sub")
    count_row = jnp.zeros((1, n_slots), jnp.float32).at[0, :LEVELS].set(
        active_counts.reshape(-1).astype(jnp.float32)
    )
    group = jnp.concatenate([targets, count_row], axis=0)
    bit = 1
    while bit < n_sub:
        group = in_order(group, xor_swap(group, "sub", bit), (me & bit) != 0)
        bit *= 2
    group_rows = group[:6]
    group_counts = group[6].reshape(n_sub, n_slots)[:, :LEVELS].reshape(-1).astype(jnp.int32)

    n_blocks = group_counts.shape[0]
    per_block = LCAP // n_sub
    offsets = (me - jnp.arange(n_blocks, dtype=jnp.int32)) % n_sub
    dealt = group_rows.reshape(6, n_blocks, per_block, n_sub)
    my_rows = jnp.take_along_axis(dealt, offsets.reshape(1, n_blocks, 1, 1), axis=3)
    my_rows = my_rows.reshape(6, n_blocks * per_block)
    my_counts = jnp.maximum(group_counts - offsets + n_sub - 1, 0) // n_sub
    my_trips = (my_counts + ROWS_PER_TRIP - 1) // ROWS_PER_TRIP

    n_local = phase.shape[1]
    have = jnp.concatenate([pred_pos, pred_vel, mass[None, :]], axis=0)
    have = have.reshape(7, n_local // LANES, LANES)
    acc = jnp.zeros((6, n_blocks * per_block, LANES), jnp.float32)
    stages = []
    bit = 1
    while bit < lax.axis_size("blk"):
        stages.append(("blk", bit))
        bit *= 2
    bit = n_sub // 2
    while bit >= 1:
        stages.append(("sub", bit))
        bit //= 2
    pending = have
    for stage, (axis, bit) in enumerate(stages):
        theirs = xor_swap(have, axis, bit)
        pending = jnp.concatenate([pending, theirs], axis=1) if pending is not None else theirs
        if stage not in WAIT_AFTER:
            acc = add_forces(my_trips, my_rows, pending, acc)
            pending = None
        have = jnp.concatenate([have, theirs], axis=1)
    my_forces = jnp.sum(acc, axis=2).reshape(6, n_blocks, per_block, 1)

    lane = lax.broadcasted_iota(jnp.int32, (1, n_blocks, 1, n_sub), 3)
    placed = jnp.where(lane == offsets.reshape(1, n_blocks, 1, 1), my_forces, 0.0)
    placed = placed.reshape(6, n_sub, n_slots)
    new_forces = lax.dynamic_index_in_dim(placed, me, axis=1, keepdims=False)
    for step in range(1, n_sub):
        outgoing = lax.dynamic_index_in_dim(placed, me ^ step, axis=1, keepdims=False)
        new_forces = new_forces + xor_swap(outgoing, "sub", step)

    shaped_forces = new_forces.reshape(6, LEVELS, LCAP)
    active_forces = jnp.where(live_grid[None, :, :], shaped_forces, jnp.zeros_like(shaped_forces))
    corrected = correct(targets, derivs[:, slot_rows], elapsed[slot_rows], new_forces)
    kept_phase = jnp.where(is_live[None, :], corrected, phase[:, slot_rows])
    kept_derivs = jnp.where(is_live[None, :], new_forces, derivs[:, slot_rows])
    new_phase = phase.at[:, slot_rows].set(kept_phase)
    new_derivs = derivs.at[:, slot_rows].set(kept_derivs)
    return (new_phase, new_derivs, active_forces)


def solution(mesh):
    in_specs = (
        P(None, ("blk", "sub")),
        P(None, ("blk", "sub")),
        P(("blk", "sub")),
        P(("blk", "sub")),
        P(None, ("blk", "sub")),
        P(None, ("blk", "sub")),
    )
    out_specs = (P(None, ("blk", "sub")), P(None, ("blk", "sub")), P(None, None, ("blk", "sub")))
    return jax.shard_map(
        on_device, mesh=mesh, in_specs=in_specs, out_specs=out_specs, check_vma=False
    )
```

```python
import jax
import jax.numpy as jnp
from jax import lax
from jax.experimental import pallas as pl
from jax.experimental.pallas import tpu as pltpu
from jax.sharding import PartitionSpec as P

LEVELS = 3
LCAP = 64
SUBLANES = 8
LANES = 128

SOFTEN_SQ = 0.0025
WAIT_AFTER = (0, 1, 3)
VPU_COST = 5000
ROWS_PER_TRIP = 1
UNROLL = 8


def predict(phase, derivs, elapsed):
    t_now = elapsed[None, :]
    pos_pred = (
        phase[:3]
        + t_now * phase[3:]
        + t_now * t_now / 2.0 * derivs[:3]
        + t_now * t_now * t_now / 6.0 * derivs[3:]
    )
    vel_pred = phase[3:] + t_now * derivs[:3] + t_now * t_now / 2.0 * derivs[3:]
    return (pos_pred, vel_pred)


def correct(pred_rows, old_rows, step_len, new_forces):
    diff_acc = old_rows[:3] - new_forces[:3]
    step_row = step_len[None, :]
    term_two = -6.0 * diff_acc - step_row * (4.0 * old_rows[3:] + 2.0 * new_forces[3:])
    term_three = 12.0 * diff_acc + 6.0 * step_row * (old_rows[3:] + new_forces[3:])
    pos_new = pred_rows[:3] + step_row * step_row * (term_two / 24.0 + term_three / 120.0)
    vel_new = pred_rows[3:] + step_row * (term_two / 6.0 + term_three / 24.0)
    return jnp.concatenate([pos_new, vel_new], axis=0)


def pair_sums(row, stars, accs):
    xi, yi, zi, ui, vi, wi = row
    xk, yk, zk, uk, vk, wk, mk = stars
    dx = xk - xi
    dy = yk - yi
    dz = zk - zi
    du = uk - ui
    dv = vk - vi
    dw = wk - wi
    dist_sq = dx * dx + dy * dy + dz * dz + SOFTEN_SQ
    inverse = lax.rsqrt(dist_sq)
    inv_sq = inverse * inverse
    weight = mk * (inv_sq * inverse)
    radial = (weight * inv_sq) * (dx * du + dy * dv + dz * dw)
    ax, ay, az, jx, jy, jz, qx, qy, qz = accs
    return (
        ax + weight * dx,
        ay + weight * dy,
        az + weight * dz,
        jx + weight * du,
        jy + weight * dv,
        jz + weight * dw,
        qx + radial * dx,
        qy + radial * dy,
        qz + radial * dz,
    )


def forces_kernel(trips_ref, rows_ref, stars_ref, acc_ref, out_ref):
    n_rows = out_ref.shape[1]
    n_blocks = trips_ref.shape[0]
    per_block = n_rows // n_blocks
    n_vregs = stars_ref.shape[1] // SUBLANES
    zero = jnp.zeros((SUBLANES, LANES), jnp.float32)
    out_ref[...] = acc_ref[...]

    def row_vectors(r):
        return tuple(rows_ref[c * n_rows + r] for c in range(6))

    for block in range(n_blocks):

        def trip_body(p, carry, block=block):
            first = block * per_block + ROWS_PER_TRIP * p
            rows = [row_vectors(first + k) for k in range(ROWS_PER_TRIP)]

            def star_body(j, accs):
                base = pl.multiple_of(j * SUBLANES, SUBLANES)
                stars = tuple(stars_ref[c, pl.ds(base, SUBLANES), :] for c in range(7))
                new = ()
                for k in range(ROWS_PER_TRIP):
                    new = new + pair_sums(rows[k], stars, accs[9 * k:9 * k + 9])
                return new

            accs = lax.fori_loop(0, n_vregs, star_body, (zero,) * (9 * ROWS_PER_TRIP), unroll=UNROLL)
            for k in range(ROWS_PER_TRIP):
                ax, ay, az, jx, jy, jz, qx, qy, qz = accs[9 * k:9 * k + 9]
                vals = (ax, ay, az, jx - 3.0 * qx, jy - 3.0 * qy, jz - 3.0 * qz)
                for c in range(6):
                    out_ref[c, pl.ds(first + k, 1), :] = out_ref[c, pl.ds(first + k, 1), :] + jnp.sum(
                        vals[c], axis=0, keepdims=True
                    )
            return carry

        lax.fori_loop(0, trips_ref[block], trip_body, 0)


def add_forces(pairs, rows, stars, acc):
    n_rows = rows.shape[1]
    n_stars = stars.shape[1] * LANES
    return pl.pallas_call(
        forces_kernel,
        out_shape=jax.ShapeDtypeStruct(acc.shape, jnp.float32),
        in_specs=[
            pl.BlockSpec(memory_space=pltpu.SMEM),
            pl.BlockSpec(memory_space=pltpu.SMEM),
            pl.BlockSpec(memory_space=pltpu.VMEM),
            pl.BlockSpec(memory_space=pltpu.VMEM),
        ],
        out_specs=pl.BlockSpec(memory_space=pltpu.VMEM),
        input_output_aliases={3: 0},
        cost_estimate=pl.CostEstimate(
            flops=VPU_COST * n_rows * n_stars,
            transcendentals=n_rows * n_stars,
            bytes_accessed=4 * (stars.size + 2 * acc.size),
        ),
    )(pairs, rows.reshape(-1), stars, acc)


def xor_swap(x, axis, bit):
    n = lax.axis_size(axis)
    return lax.ppermute(x, axis, [(i, i ^ bit) for i in range(n)])


def in_order(mine, theirs, upper):
    return jnp.where(upper, jnp.concatenate([theirs, mine], axis=1), jnp.concatenate([mine, theirs], axis=1))


def on_device(phase, derivs, mass, elapsed, active_slots, active_counts):
    pred_pos, pred_vel = predict(phase, derivs, elapsed)
    slot_rows = active_slots.reshape(-1)
    live_grid = lax.broadcasted_iota(jnp.int32, (LEVELS, LCAP), 1) < active_counts
    is_live = live_grid.reshape(-1)
    targets = jnp.concatenate([pred_pos[:, slot_rows], pred_vel[:, slot_rows]], axis=0)
    n_slots = targets.shape[1]

    n_sub = lax.axis_size("sub")
    me = lax.axis_index("sub")
    count_row = jnp.zeros((1, n_slots), jnp.float32).at[0, :LEVELS].set(
        active_counts.reshape(-1).astype(jnp.float32)
    )
    group = jnp.concatenate([targets, count_row], axis=0)
    bit = 1
    while bit < n_sub:
        group = in_order(group, xor_swap(group, "sub", bit), (me & bit) != 0)
        bit *= 2
    group_rows = group[:6]
    group_counts = group[6].reshape(n_sub, n_slots)[:, :LEVELS].reshape(-1).astype(jnp.int32)

    n_blocks = group_counts.shape[0]
    per_block = LCAP // n_sub
    offsets = (me - jnp.arange(n_blocks, dtype=jnp.int32)) % n_sub
    dealt = group_rows.reshape(6, n_blocks, per_block, n_sub)
    my_rows = jnp.take_along_axis(dealt, offsets.reshape(1, n_blocks, 1, 1), axis=3)
    my_rows = my_rows.reshape(6, n_blocks * per_block)
    my_counts = jnp.maximum(group_counts - offsets + n_sub - 1, 0) // n_sub
    my_trips = (my_counts + ROWS_PER_TRIP - 1) // ROWS_PER_TRIP

    n_local = phase.shape[1]
    have = jnp.concatenate([pred_pos, pred_vel, mass[None, :]], axis=0)
    have = have.reshape(7, n_local // LANES, LANES)
    acc = jnp.zeros((6, n_blocks * per_block, LANES), jnp.float32)
    stages = []
    bit = 1
    while bit < lax.axis_size("blk"):
        stages.append(("blk", bit))
        bit *= 2
    bit = n_sub // 2
    while bit >= 1:
        stages.append(("sub", bit))
        bit //= 2
    pending = have
    for stage, (axis, bit) in enumerate(stages):
        theirs = xor_swap(have, axis, bit)
        pending = jnp.concatenate([pending, theirs], axis=1) if pending is not None else theirs
        if stage not in WAIT_AFTER:
            acc = add_forces(my_trips, my_rows, pending, acc)
            pending = None
        have = jnp.concatenate([have, theirs], axis=1)
    my_forces = jnp.sum(acc, axis=2).reshape(6, n_blocks, per_block, 1)

    lane = lax.broadcasted_iota(jnp.int32, (1, n_blocks, 1, n_sub), 3)
    placed = jnp.where(lane == offsets.reshape(1, n_blocks, 1, 1), my_forces, 0.0)
    placed = placed.reshape(6, n_sub, n_slots)
    new_forces = lax.dynamic_index_in_dim(placed, me, axis=1, keepdims=False)
    for step in range(1, n_sub):
        outgoing = lax.dynamic_index_in_dim(placed, me ^ step, axis=1, keepdims=False)
        new_forces = new_forces + xor_swap(outgoing, "sub", step)

    shaped_forces = new_forces.reshape(6, LEVELS, LCAP)
    active_forces = jnp.where(live_grid[None, :, :], shaped_forces, jnp.zeros_like(shaped_forces))
    corrected = correct(targets, derivs[:, slot_rows], elapsed[slot_rows], new_forces)
    kept_phase = jnp.where(is_live[None, :], corrected, phase[:, slot_rows])
    kept_derivs = jnp.where(is_live[None, :], new_forces, derivs[:, slot_rows])
    new_phase = phase.at[:, slot_rows].set(kept_phase)
    new_derivs = derivs.at[:, slot_rows].set(kept_derivs)
    return (new_phase, new_derivs, active_forces)


def solution(mesh):
    in_specs = (
        P(None, ("blk", "sub")),
        P(None, ("blk", "sub")),
        P(("blk", "sub")),
        P(("blk", "sub")),
        P(None, ("blk", "sub")),
        P(None, ("blk", "sub")),
    )
    out_specs = (P(None, ("blk", "sub")), P(None, ("blk", "sub")), P(None, None, ("blk", "sub")))
    return jax.shard_map(
        on_device, mesh=mesh, in_specs=in_specs, out_specs=out_specs, check_vma=False
    )
```

```python
import jax
import jax.numpy as jnp
from jax import lax
from jax.experimental import pallas as pl
from jax.experimental.pallas import tpu as pltpu
from jax.sharding import PartitionSpec as P

LEVELS = 3
LCAP = 64
SUBLANES = 8
LANES = 128

SOFTEN_SQ = 0.0025
MIN_ROWS = 64
VPU_COST = 5000
ROWS_PER_TRIP = 1
UNROLL = 6


def predict(phase, derivs, elapsed):
    t_now = elapsed[None, :]
    pos_pred = (
        phase[:3]
        + t_now * phase[3:]
        + t_now * t_now / 2.0 * derivs[:3]
        + t_now * t_now * t_now / 6.0 * derivs[3:]
    )
    vel_pred = phase[3:] + t_now * derivs[:3] + t_now * t_now / 2.0 * derivs[3:]
    return (pos_pred, vel_pred)


def correct(pred_rows, old_rows, step_len, new_forces):
    diff_acc = old_rows[:3] - new_forces[:3]
    step_row = step_len[None, :]
    term_two = -6.0 * diff_acc - step_row * (4.0 * old_rows[3:] + 2.0 * new_forces[3:])
    term_three = 12.0 * diff_acc + 6.0 * step_row * (old_rows[3:] + new_forces[3:])
    pos_new = pred_rows[:3] + step_row * step_row * (term_two / 24.0 + term_three / 120.0)
    vel_new = pred_rows[3:] + step_row * (term_two / 6.0 + term_three / 24.0)
    return jnp.concatenate([pos_new, vel_new], axis=0)


def pair_sums(row, stars, accs):
    xi, yi, zi, ui, vi, wi = row
    xk, yk, zk, uk, vk, wk, mk = stars
    dx = xk - xi
    dy = yk - yi
    dz = zk - zi
    du = uk - ui
    dv = vk - vi
    dw = wk - wi
    dist_sq = dx * dx + dy * dy + dz * dz + SOFTEN_SQ
    inverse = lax.rsqrt(dist_sq)
    inv_sq = inverse * inverse
    weight = mk * (inv_sq * inverse)
    radial = (weight * inv_sq) * (dx * du + dy * dv + dz * dw)
    ax, ay, az, jx, jy, jz, qx, qy, qz = accs
    return (
        ax + weight * dx,
        ay + weight * dy,
        az + weight * dz,
        jx + weight * du,
        jy + weight * dv,
        jz + weight * dw,
        qx + radial * dx,
        qy + radial * dy,
        qz + radial * dz,
    )


def forces_kernel(trips_ref, rows_ref, stars_ref, acc_ref, out_ref):
    n_rows = out_ref.shape[1]
    n_blocks = trips_ref.shape[0]
    per_block = n_rows // n_blocks
    n_vregs = stars_ref.shape[1] // SUBLANES
    zero = jnp.zeros((SUBLANES, LANES), jnp.float32)
    out_ref[...] = acc_ref[...]

    def row_vectors(r):
        return tuple(rows_ref[c * n_rows + r] for c in range(6))

    for block in range(n_blocks):

        def trip_body(p, carry, block=block):
            first = block * per_block + ROWS_PER_TRIP * p
            rows = [row_vectors(first + k) for k in range(ROWS_PER_TRIP)]

            def star_body(j, accs):
                base = pl.multiple_of(j * SUBLANES, SUBLANES)
                stars = tuple(stars_ref[c, pl.ds(base, SUBLANES), :] for c in range(7))
                new = ()
                for k in range(ROWS_PER_TRIP):
                    new = new + pair_sums(rows[k], stars, accs[9 * k:9 * k + 9])
                return new

            accs = lax.fori_loop(0, n_vregs, star_body, (zero,) * (9 * ROWS_PER_TRIP), unroll=UNROLL)
            for k in range(ROWS_PER_TRIP):
                ax, ay, az, jx, jy, jz, qx, qy, qz = accs[9 * k:9 * k + 9]
                vals = (ax, ay, az, jx - 3.0 * qx, jy - 3.0 * qy, jz - 3.0 * qz)
                for c in range(6):
                    out_ref[c, pl.ds(first + k, 1), :] = out_ref[c, pl.ds(first + k, 1), :] + jnp.sum(
                        vals[c], axis=0, keepdims=True
                    )
            return carry

        lax.fori_loop(0, trips_ref[block], trip_body, 0)


def add_forces(pairs, rows, stars, acc):
    n_rows = rows.shape[1]
    n_stars = stars.shape[1] * LANES
    return pl.pallas_call(
        forces_kernel,
        out_shape=jax.ShapeDtypeStruct(acc.shape, jnp.float32),
        in_specs=[
            pl.BlockSpec(memory_space=pltpu.SMEM),
            pl.BlockSpec(memory_space=pltpu.SMEM),
            pl.BlockSpec(memory_space=pltpu.VMEM),
            pl.BlockSpec(memory_space=pltpu.VMEM),
        ],
        out_specs=pl.BlockSpec(memory_space=pltpu.VMEM),
        input_output_aliases={3: 0},
        cost_estimate=pl.CostEstimate(
            flops=VPU_COST * n_rows * n_stars,
            transcendentals=n_rows * n_stars,
            bytes_accessed=4 * (stars.size + 2 * acc.size),
        ),
    )(pairs, rows.reshape(-1), stars, acc)


def xor_swap(x, axis, bit):
    n = lax.axis_size(axis)
    return lax.ppermute(x, axis, [(i, i ^ bit) for i in range(n)])


def in_order(mine, theirs, upper):
    return jnp.where(upper, jnp.concatenate([theirs, mine], axis=1), jnp.concatenate([mine, theirs], axis=1))


def on_device(phase, derivs, mass, elapsed, active_slots, active_counts):
    pred_pos, pred_vel = predict(phase, derivs, elapsed)
    slot_rows = active_slots.reshape(-1)
    live_grid = lax.broadcasted_iota(jnp.int32, (LEVELS, LCAP), 1) < active_counts
    is_live = live_grid.reshape(-1)
    targets = jnp.concatenate([pred_pos[:, slot_rows], pred_vel[:, slot_rows]], axis=0)
    n_slots = targets.shape[1]

    n_sub = lax.axis_size("sub")
    me = lax.axis_index("sub")
    count_row = jnp.zeros((1, n_slots), jnp.float32).at[0, :LEVELS].set(
        active_counts.reshape(-1).astype(jnp.float32)
    )
    group = jnp.concatenate([targets, count_row], axis=0)
    bit = 1
    while bit < n_sub:
        group = in_order(group, xor_swap(group, "sub", bit), (me & bit) != 0)
        bit *= 2
    group_rows = group[:6]
    group_counts = group[6].reshape(n_sub, n_slots)[:, :LEVELS].reshape(-1).astype(jnp.int32)

    n_blocks = group_counts.shape[0]
    per_block = LCAP // n_sub
    offsets = (me - jnp.arange(n_blocks, dtype=jnp.int32)) % n_sub
    dealt = group_rows.reshape(6, n_blocks, per_block, n_sub)
    my_rows = jnp.take_along_axis(dealt, offsets.reshape(1, n_blocks, 1, 1), axis=3)
    my_rows = my_rows.reshape(6, n_blocks * per_block)
    my_counts = jnp.maximum(group_counts - offsets + n_sub - 1, 0) // n_sub
    my_trips = (my_counts + ROWS_PER_TRIP - 1) // ROWS_PER_TRIP

    n_local = phase.shape[1]
    have = jnp.concatenate([pred_pos, pred_vel, mass[None, :]], axis=0)
    have = have.reshape(7, n_local // LANES, LANES)
    acc = jnp.zeros((6, n_blocks * per_block, LANES), jnp.float32)
    stages = []
    bit = 1
    while bit < lax.axis_size("blk"):
        stages.append(("blk", bit))
        bit *= 2
    bit = n_sub // 2
    while bit >= 1:
        stages.append(("sub", bit))
        bit //= 2
    pending = None
    for axis, bit in stages:
        theirs = xor_swap(have, axis, bit)
        if pending is None and have.shape[1] + theirs.shape[1] >= MIN_ROWS:
            pending = jnp.concatenate([have, theirs], axis=1)
        elif pending is not None:
            pending = theirs
        if pending is not None:
            acc = add_forces(my_trips, my_rows, pending, acc)
        have = jnp.concatenate([have, theirs], axis=1)
    my_forces = jnp.sum(acc, axis=2).reshape(6, n_blocks, per_block, 1)

    lane = lax.broadcasted_iota(jnp.int32, (1, n_blocks, 1, n_sub), 3)
    placed = jnp.where(lane == offsets.reshape(1, n_blocks, 1, 1), my_forces, 0.0)
    placed = placed.reshape(6, n_sub, n_slots)
    new_forces = lax.dynamic_index_in_dim(placed, me, axis=1, keepdims=False)
    for step in range(1, n_sub):
        outgoing = lax.dynamic_index_in_dim(placed, me ^ step, axis=1, keepdims=False)
        new_forces = new_forces + xor_swap(outgoing, "sub", step)

    shaped_forces = new_forces.reshape(6, LEVELS, LCAP)
    active_forces = jnp.where(live_grid[None, :, :], shaped_forces, jnp.zeros_like(shaped_forces))
    corrected = correct(targets, derivs[:, slot_rows], elapsed[slot_rows], new_forces)
    kept_phase = jnp.where(is_live[None, :], corrected, phase[:, slot_rows])
    kept_derivs = jnp.where(is_live[None, :], new_forces, derivs[:, slot_rows])
    new_phase = phase.at[:, slot_rows].set(kept_phase)
    new_derivs = derivs.at[:, slot_rows].set(kept_derivs)
    return (new_phase, new_derivs, active_forces)


def solution(mesh):
    in_specs = (
        P(None, ("blk", "sub")),
        P(None, ("blk", "sub")),
        P(("blk", "sub")),
        P(("blk", "sub")),
        P(None, ("blk", "sub")),
        P(None, ("blk", "sub")),
    )
    out_specs = (P(None, ("blk", "sub")), P(None, ("blk", "sub")), P(None, None, ("blk", "sub")))
    return jax.shard_map(
        on_device, mesh=mesh, in_specs=in_specs, out_specs=out_specs, check_vma=False
    )
```
